512 devices in a mesh: op: 16 (over y, core), sec: 32 (over x, z).
Axes of the slice: x: 4, y: 8, z: 8, core: 2. Of those that a mesh axis runs over, the one named last changes fastest.
Arguments:
- wavefunction: bfloat16 [128, 64, 1024], P('sec'), may hold values from -6 to 6
- left_env: bfloat16 [128, 128, 64, 64], P('op', 'sec'), may hold values from -0.75 to 0.75
- right_env: bfloat16 [64, 128, 64, 64], P('op', 'sec'), may hold values from -0.75 to 0.75
- local_ops: bfloat16 [128, 4, 16, 16], P('op'), may hold values from -0.0625 to 0.0625
- dest_sector: int32 [128, 128], P('op'), may hold values from 0 to 127, as said below
- right_bond: int32 [128, 4], P('op'), may hold values from 0 to 3
Outputs:
- new_vector: bfloat16 [128, 64, 1024], P('sec', 'op')
The draws below stay inside these ranges and needn't reach their ends.
Inputs may be any that keep to these rules, and one draw needn't show every extreme that they name: `dest_sector`: for each operator group (rows a with equal a // 8) and each block of 4 source sectors, exactly 1 of those 32 entries fall into each block of 4 destination sectors.
All inputs are finite; a program needn't handle non-finite values.
Results may differ from the reference program's by a relative error of at most 0.018.
Values may be sent and summed in bfloat16 or wider, within the bound.
No kernel may reach another device: no remote copies, remote signals or barrier semaphores. Data moves between devices by JAX's collectives and lax.ppermute only.
A program may use at most 128 MiB of HBM per device.

```python
import jax
import jax.numpy as jnp
from jax import lax

BS = 64
PH = 16
S_DEV = 4
A_DEV = 8
B_DEV = 4
TPA = 4
S = 128
A = 128
RB = 64


def draw_dest_sector(key, part):
    group_count = A // A_DEV
    block_count = S // S_DEV
    per_block = A_DEV * S_DEV // block_count
    pair_count = A_DEV * S_DEV
    keys = jax.random.split(jax.random.fold_in(key, 11), group_count * block_count)
    shuffled = jax.vmap(lambda one_key: jax.random.permutation(one_key, pair_count))(keys)
    target_block = shuffled // per_block
    inside = jax.random.randint(jax.random.fold_in(key, 12), (group_count * block_count, pair_count), 0, S_DEV)
    flat = (target_block * S_DEV + inside).astype(jnp.int32)
    flat = flat.reshape(group_count, block_count, A_DEV, S_DEV)
    return flat.transpose(0, 2, 1, 3).reshape(A, S)


def touch_ends(entries, stream_key, least, top_value):
    spot = [jax.random.randint(jax.random.fold_in(stream_key, axis), (), 0, length) for axis, length in enumerate(entries.shape)]
    longest = entries.shape.index(max(entries.shape))
    next_to = spot[:longest] + [(spot[longest] + 1) % entries.shape[longest]] + spot[longest + 1:]
    return entries.at[tuple(spot)].set(least).at[tuple(next_to)].set(top_value)


def shard_levels(own_key, extent, cuts, low, largest):
    level = 1.0
    for axis_at, shards_of in cuts:
        draws = jax.random.uniform(jax.random.fold_in(jax.random.fold_in(own_key, 6), axis_at), (shards_of,), jnp.float32, low / len(cuts), largest / len(cuts))
        level = level * jnp.repeat(jnp.exp(draws), extent[axis_at] // shards_of).reshape((-1,) + (1,) * (len(extent) - 1 - axis_at))
    return level


def scatter_about(stream_key, extent, spread, limit, pieces=(), held_as=jnp.bfloat16):
    values = spread * jax.random.normal(stream_key, extent, jnp.float32)
    if pieces:
        values = values * shard_levels(stream_key, extent, pieces, -0.22, 0.18)
    return jnp.clip(values, -limit, limit).astype(held_as)


def setup_inputs(seed: int = 0) -> dict:
    key_of = jax.random.split(jax.random.key(seed), 7)
    wavefunction = scatter_about(key_of[0], (S, BS, PH * BS), 1.0, 6.0, ((0, 32),))
    left_env = scatter_about(key_of[1], (A, S, BS, BS), BS ** -0.5, 0.75, ((0, 16), (1, 32)))
    right_env = scatter_about(key_of[2], (RB, S, BS, BS), BS ** -0.5, 0.75, ((0, 16), (1, 32)))
    local_ops = scatter_about(key_of[3], (A, TPA, PH, PH), (PH * TPA * A) ** -0.5, 0.0625, ((0, 16),))
    dest_sector = draw_dest_sector(jax.random.fold_in(key_of[6], 71), 0)
    right_bond = touch_ends(jax.random.randint(key_of[5], (A, TPA), 0, B_DEV), jax.random.fold_in(key_of[5], 1), 0, B_DEV - 1).astype(jnp.int32)
    return dict(wavefunction=wavefunction, left_env=left_env, right_env=right_env, local_ops=local_ops, dest_sector=dest_sector, right_bond=right_bond)


def group_term(wavefunction, left_env, right_env, local_ops, dest_sector, right_bond, group):
    start = (group * A_DEV).astype(jnp.int32)
    left = lax.dynamic_slice_in_dim(left_env, start, A_DEV, 0)
    ops_here = lax.dynamic_slice_in_dim(local_ops, start, A_DEV, 0)
    dest_here = lax.dynamic_slice_in_dim(dest_sector, start, A_DEV, 0)
    bonds_here = lax.dynamic_slice_in_dim(right_bond, start, A_DEV, 0)
    right_here = lax.dynamic_slice_in_dim(right_env, (group * B_DEV).astype(jnp.int32), B_DEV, 0)
    moved = jnp.einsum('asij,sjx->asix', left.astype(jnp.float32), wavefunction.astype(jnp.float32)).astype(jnp.bfloat16)
    moved = moved.reshape(A_DEV, S, BS, PH, BS)
    accum = jnp.zeros((A_DEV, S, BS, PH, BS), jnp.float32)
    for term_index in range(TPA):
        mixed = jnp.einsum('apq,aslqr->aslpr', ops_here[:, term_index].astype(jnp.float32), moved.astype(jnp.float32)).astype(jnp.bfloat16)
        chosen = right_here[bonds_here[:, term_index][:, None], dest_here]
        accum = accum + jnp.einsum('aslpr,asmr->aslpm', mixed.astype(jnp.float32), chosen.astype(jnp.float32))
    partial_value = jax.ops.segment_sum(accum.reshape(A_DEV * S, BS * PH * BS), dest_here.reshape(A_DEV * S), num_segments=S)
    rounded = lax.optimization_barrier(partial_value.astype(jnp.bfloat16))
    return rounded.astype(jnp.float32)


def reference(wavefunction, left_env, right_env, local_ops, dest_sector, right_bond):
    def step(carry, group):
        return carry + group_term(wavefunction, left_env, right_env, local_ops, dest_sector, right_bond, group), None

    start_sum = jnp.zeros((S, BS * PH * BS), jnp.float32)
    applied, unused = lax.scan(step, start_sum, jnp.arange(A // A_DEV, dtype=jnp.int32))
    return applied.reshape(S, BS, PH * BS).astype(jnp.bfloat16)
```

```python
import jax
import jax.numpy as jnp
from jax import lax
from jax.sharding import PartitionSpec as P


def body(wavefunction, left_env, right_env, local_ops, dest_sector, right_bond):
    sec_blocks, rows, width = wavefunction.shape
    left_count = left_env.shape[0]
    right_count = right_env.shape[0]
    terms = local_ops.shape[1]
    physical = width // rows
    sec_count = lax.axis_size("sec")
    op_count = lax.axis_size("op")
    own_sec = lax.axis_index("sec")
    f32 = jnp.float32
    bf16 = jnp.bfloat16

    own_dest = lax.dynamic_slice_in_dim(dest_sector, own_sec * sec_blocks, sec_blocks, 1)
    target = own_dest // sec_blocks
    peers = jnp.arange(sec_count, dtype=jnp.int32)
    send_hot = (target[:, :, None] == peers[None, None, :]).astype(bf16)
    chosen_left = jnp.einsum(
        "ask,asij->kisj", send_hot, left_env, preferred_element_type=f32
    ).astype(bf16)
    outgoing = jnp.einsum(
        "kisj,sjx->kix", chosen_left, wavefunction, preferred_element_type=f32
    ).astype(bf16)
    incoming = lax.all_to_all(outgoing, "sec", 0, 0, tiled=True)
    incoming = incoming.reshape(sec_count, rows, physical, rows)

    grid = dest_sector.reshape(left_count, sec_count, sec_blocks)
    mine = (grid // sec_blocks) == own_sec
    bond_hot = jnp.sum(mine, axis=2).T.astype(bf16)
    local_dest = jnp.sum(jnp.where(mine, grid % sec_blocks, 0), axis=(0, 2))
    dest_hot = local_dest[:, None] == jnp.arange(sec_blocks, dtype=jnp.int32)[None, :]
    item_ops = jnp.einsum(
        "ia,atpq->itpq", bond_hot, local_ops, preferred_element_type=f32
    ).astype(bf16)
    item_bond = jnp.einsum(
        "ia,at->it", bond_hot.astype(f32), right_bond.astype(f32)
    ).astype(jnp.int32)
    env_hot = (
        (item_bond[:, :, None, None] == jnp.arange(right_count, dtype=jnp.int32)[None, None, :, None])
        & dest_hot[:, None, None, :]
    ).astype(bf16)
    item_env = jnp.einsum(
        "itbd,bdmr->itmr", env_hot, right_env, preferred_element_type=f32
    ).astype(bf16)
    mixed = jnp.einsum(
        "itpq,ilqr->itlpr", item_ops, incoming, preferred_element_type=f32
    ).astype(bf16)
    accum = jnp.einsum("itlpr,itmr->ilpm", mixed, item_env, preferred_element_type=f32)
    partial_value = jnp.einsum(
        "id,ilpm->dlpm",
        dest_hot.astype(f32),
        accum,
        precision=lax.Precision.HIGHEST,
        preferred_element_type=f32,
    )
    share = rows // op_count
    pieces = partial_value.astype(bf16).reshape(sec_blocks, op_count, share, width)
    pieces = pieces.transpose(1, 0, 2, 3)
    gathered = lax.all_to_all(pieces, "op", 0, 0, tiled=True)
    summed = jnp.sum(gathered.astype(f32), axis=0)
    return summed.astype(bf16)


def solution(mesh):
    return jax.shard_map(
        body,
        mesh=mesh,
        in_specs=(
            P("sec", None, None),
            P("op", "sec", None, None),
            P("op", "sec", None, None),
            P("op", None, None, None),
            P("op", None),
            P("op", None),
        ),
        out_specs=P("sec", "op", None),
        check_vma=False,
    )
```

```python
import jax
import jax.numpy as jnp
from jax import lax
from jax.sharding import PartitionSpec as P


CHUNKS = 4


def body(wavefunction, left_env, right_env, local_ops, dest_sector, right_bond):
    sec_blocks, rows, width = wavefunction.shape
    left_count = left_env.shape[0]
    right_count = right_env.shape[0]
    terms = local_ops.shape[1]
    physical = width // rows
    sec_count = lax.axis_size("sec")
    op_count = lax.axis_size("op")
    own_sec = lax.axis_index("sec")
    f32 = jnp.float32
    bf16 = jnp.bfloat16

    own_dest = lax.dynamic_slice_in_dim(dest_sector, own_sec * sec_blocks, sec_blocks, 1)
    target = own_dest // sec_blocks
    peers = jnp.arange(sec_count, dtype=jnp.int32)
    send_hot = (target[:, :, None] == peers[None, None, :]).astype(bf16)
    chosen_left = jnp.einsum(
        "ask,asij->kisj", send_hot, left_env, preferred_element_type=f32
    ).astype(bf16)
    outgoing = jnp.einsum(
        "kisj,sjx->kix", chosen_left, wavefunction, preferred_element_type=f32
    ).astype(bf16)
    grid = dest_sector.reshape(left_count, sec_count, sec_blocks)
    mine = (grid // sec_blocks) == own_sec
    bond_hot = jnp.sum(mine, axis=2).T.astype(bf16)
    local_dest = jnp.sum(jnp.where(mine, grid % sec_blocks, 0), axis=(0, 2))
    dest_hot = local_dest[:, None] == jnp.arange(sec_blocks, dtype=jnp.int32)[None, :]
    item_ops = jnp.einsum(
        "ia,atpq->itpq", bond_hot, local_ops, preferred_element_type=f32
    ).astype(bf16)
    item_bond = jnp.einsum(
        "ia,at->it", bond_hot.astype(f32), right_bond.astype(f32)
    ).astype(jnp.int32)
    env_hot = (
        (item_bond[:, :, None, None] == jnp.arange(right_count, dtype=jnp.int32)[None, None, :, None])
        & dest_hot[:, None, None, :]
    ).astype(bf16)
    item_env = jnp.einsum(
        "itbd,bdmr->itmr", env_hot, right_env, preferred_element_type=f32
    ).astype(bf16)

    chunk = rows // CHUNKS
    def process(received):
        incoming = received.reshape(sec_count, chunk, physical, rows)
        mixed = jnp.einsum(
            "itpq,ilqr->itlpr", item_ops, incoming, preferred_element_type=f32
        ).astype(bf16)
        accum = jnp.einsum("itlpr,itmr->ilpm", mixed, item_env, preferred_element_type=f32)
        return jnp.stack(
            [
                jnp.sum(jnp.where(dest_hot[:, d, None, None, None], accum, 0.0), axis=0)
                for d in range(sec_blocks)
            ]
        )

    def send(c):
        return lax.all_to_all(outgoing[:, c * chunk:(c + 1) * chunk], "sec", 0, 0, tiled=True)

    received = send(0)
    parts = []
    for c in range(CHUNKS):
        upcoming = None
        if c + 1 < CHUNKS:
            piece = outgoing[:, (c + 1) * chunk:(c + 2) * chunk]
            if parts:
                piece, parts[-1] = lax.optimization_barrier((piece, parts[-1]))
            upcoming = lax.all_to_all(piece, "sec", 0, 0, tiled=True)
        parts.append(process(received))
        received = upcoming
    partial_value = jnp.concatenate(parts, axis=1)
    share = rows // op_count
    pieces = partial_value.astype(bf16).reshape(sec_blocks, op_count, share, width)
    pieces = pieces.transpose(1, 0, 2, 3)
    gathered = lax.all_to_all(pieces, "op", 0, 0, tiled=True)
    summed = jnp.sum(gathered.astype(f32), axis=0)
    return summed.astype(bf16)


def solution(mesh):
    return jax.shard_map(
        body,
        mesh=mesh,
        in_specs=(
            P("sec", None, None),
            P("op", "sec", None, None),
            P("op", "sec", None, None),
            P("op", None, None, None),
            P("op", None),
            P("op", None),
        ),
        out_specs=P("sec", "op", None),
        check_vma=False,
    )
```

```python
import jax
import jax.numpy as jnp
from jax import lax
from jax.sharding import PartitionSpec as P


CHUNKS = 2


def body(wavefunction, left_env, right_env, local_ops, dest_sector, right_bond):
    sec_blocks, rows, width = wavefunction.shape
    left_count = left_env.shape[0]
    right_count = right_env.shape[0]
    terms = local_ops.shape[1]
    physical = width // rows
    sec_count = lax.axis_size("sec")
    op_count = lax.axis_size("op")
    own_sec = lax.axis_index("sec")
    f32 = jnp.float32
    bf16 = jnp.bfloat16

    own_dest = lax.dynamic_slice_in_dim(dest_sector, own_sec * sec_blocks, sec_blocks, 1)
    target = own_dest // sec_blocks
    peers = jnp.arange(sec_count, dtype=jnp.int32)
    send_hot = (target[:, :, None] == peers[None, None, :]).astype(bf16)
    chosen_left = jnp.einsum(
        "ask,asij->kisj", send_hot, left_env, preferred_element_type=f32
    ).astype(bf16)
    outgoing = jnp.einsum(
        "kisj,sjx->kix", chosen_left, wavefunction, preferred_element_type=f32
    ).astype(bf16)
    grid = dest_sector.reshape(left_count, sec_count, sec_blocks)
    mine = (grid // sec_blocks) == own_sec
    bond_hot = jnp.sum(mine, axis=2).T.astype(bf16)
    local_dest = jnp.sum(jnp.where(mine, grid % sec_blocks, 0), axis=(0, 2))
    dest_hot = local_dest[:, None] == jnp.arange(sec_blocks, dtype=jnp.int32)[None, :]
    item_ops = jnp.einsum(
        "ia,atpq->itpq", bond_hot, local_ops, preferred_element_type=f32
    ).astype(bf16)
    item_bond = jnp.einsum(
        "ia,at->it", bond_hot.astype(f32), right_bond.astype(f32)
    ).astype(jnp.int32)
    env_hot = (
        (item_bond[:, :, None, None] == jnp.arange(right_count, dtype=jnp.int32)[None, None, :, None])
        & dest_hot[:, None, None, :]
    ).astype(bf16)
    item_env = jnp.einsum(
        "itbd,bdmr->itmr", env_hot, right_env, preferred_element_type=f32
    ).astype(bf16)

    chunk = rows // CHUNKS
    def process(received):
        incoming = received.reshape(sec_count, chunk, physical, rows)
        mixed = jnp.einsum(
            "itpq,ilqr->itlpr", item_ops, incoming, preferred_element_type=f32
        ).astype(bf16)
        accum = jnp.einsum("itlpr,itmr->ilpm", mixed, item_env, preferred_element_type=f32)
        return jnp.stack(
            [
                jnp.sum(jnp.where(dest_hot[:, d, None, None, None], accum, 0.0), axis=0)
                for d in range(sec_blocks)
            ]
        )

    def send(c):
        return lax.all_to_all(outgoing[:, c * chunk:(c + 1) * chunk], "sec", 0, 0, tiled=True)

    received = send(0)
    parts = []
    for c in range(CHUNKS):
        upcoming = None
        if c + 1 < CHUNKS:
            piece = outgoing[:, (c + 1) * chunk:(c + 2) * chunk]
            if parts:
                piece, parts[-1] = lax.optimization_barrier((piece, parts[-1]))
            upcoming = lax.all_to_all(piece, "sec", 0, 0, tiled=True)
        parts.append(process(received))
        received = upcoming
    partial_value = jnp.concatenate(parts, axis=1)
    share = rows // op_count
    pieces = partial_value.astype(bf16).reshape(sec_blocks, op_count, share, width)
    pieces = pieces.transpose(1, 0, 2, 3)
    gathered = lax.all_to_all(pieces, "op", 0, 0, tiled=True)
    summed = jnp.sum(gathered.astype(f32), axis=0)
    return summed.astype(bf16)


def solution(mesh):
    return jax.shard_map(
        body,
        mesh=mesh,
        in_specs=(
            P("sec", None, None),
            P("op", "sec", None, None),
            P("op", "sec", None, None),
            P("op", None, None, None),
            P("op", None),
            P("op", None),
        ),
        out_specs=P("sec", "op", None),
        check_vma=False,
    )
```

```python
import jax
import jax.numpy as jnp
from jax import lax
from jax.sharding import PartitionSpec as P


CHUNKS = 2


def body(wavefunction, left_env, right_env, local_ops, dest_sector, right_bond):
    sec_blocks, rows, width = wavefunction.shape
    left_count = left_env.shape[0]
    right_count = right_env.shape[0]
    terms = local_ops.shape[1]
    physical = width // rows
    sec_count = lax.axis_size("sec")
    op_count = lax.axis_size("op")
    own_sec = lax.axis_index("sec")
    f32 = jnp.float32
    bf16 = jnp.bfloat16

    own_dest = lax.dynamic_slice_in_dim(dest_sector, own_sec * sec_blocks, sec_blocks, 1)
    target = own_dest // sec_blocks
    peers = jnp.arange(sec_count, dtype=jnp.int32)
    send_hot = (target[:, :, None] == peers[None, None, :]).astype(bf16)
    chosen_left = jnp.einsum(
        "ask,asij->kisj", send_hot, left_env, preferred_element_type=f32
    ).astype(bf16)
    outgoing = jnp.einsum(
        "kisj,sjx->kix", chosen_left, wavefunction, preferred_element_type=f32
    ).astype(bf16)
    grid = dest_sector.reshape(left_count, sec_count, sec_blocks)
    mine = (grid // sec_blocks) == own_sec
    bond_hot = jnp.sum(mine, axis=2).T.astype(bf16)
    local_dest = jnp.sum(jnp.where(mine, grid % sec_blocks, 0), axis=(0, 2))
    dest_hot = local_dest[:, None] == jnp.arange(sec_blocks, dtype=jnp.int32)[None, :]
    item_ops = jnp.einsum(
        "ia,atpq->itpq", bond_hot, local_ops, preferred_element_type=f32
    ).astype(bf16)
    item_bond = jnp.einsum(
        "ia,at->it", bond_hot.astype(f32), right_bond.astype(f32)
    ).astype(jnp.int32)
    env_hot = (
        (item_bond[:, :, None, None] == jnp.arange(right_count, dtype=jnp.int32)[None, None, :, None])
        & dest_hot[:, None, None, :]
    ).astype(bf16)
    item_env = jnp.einsum(
        "itbd,bdmr->itmr", env_hot, right_env, preferred_element_type=f32
    ).astype(bf16)

    sector_env = jnp.einsum(
        "itmr,id->itdmr", item_env, dest_hot.astype(bf16), preferred_element_type=f32
    ).astype(bf16)

    chunk = rows // CHUNKS
    def process(received):
        incoming = received.reshape(sec_count, chunk, physical, rows)
        mixed = jnp.einsum(
            "itpq,ilqr->itlpr", item_ops, incoming, preferred_element_type=f32
        ).astype(bf16)
        return jnp.einsum("itlpr,itdmr->dlpm", mixed, sector_env, preferred_element_type=f32)

    def send(c):
        return lax.all_to_all(outgoing[:, c * chunk:(c + 1) * chunk], "sec", 0, 0, tiled=True)

    received = send(0)
    parts = []
    for c in range(CHUNKS):
        upcoming = None
        if c + 1 < CHUNKS:
            piece = outgoing[:, (c + 1) * chunk:(c + 2) * chunk]
            if parts:
                piece, parts[-1] = lax.optimization_barrier((piece, parts[-1]))
            upcoming = lax.all_to_all(piece, "sec", 0, 0, tiled=True)
        parts.append(process(received))
        received = upcoming
    partial_value = jnp.concatenate(parts, axis=1)
    share = rows // op_count
    pieces = partial_value.astype(bf16).reshape(sec_blocks, op_count, share, width)
    pieces = pieces.transpose(1, 0, 2, 3)
    gathered = lax.all_to_all(pieces, "op", 0, 0, tiled=True)
    summed = jnp.sum(gathered.astype(f32), axis=0)
    return summed.astype(bf16)


def solution(mesh):
    return jax.shard_map(
        body,
        mesh=mesh,
        in_specs=(
            P("sec", None, None),
            P("op", "sec", None, None),
            P("op", "sec", None, None),
            P("op", None, None, None),
            P("op", None),
            P("op", None),
        ),
        out_specs=P("sec", "op", None),
        check_vma=False,
    )
```

```python
import jax
import jax.numpy as jnp
from jax import lax
from jax.sharding import PartitionSpec as P


CHUNKS = 4


def body(wavefunction, left_env, right_env, local_ops, dest_sector, right_bond):
    sec_blocks, rows, width = wavefunction.shape
    left_count = left_env.shape[0]
    right_count = right_env.shape[0]
    terms = local_ops.shape[1]
    physical = width // rows
    sec_count = lax.axis_size("sec")
    op_count = lax.axis_size("op")
    own_sec = lax.axis_index("sec")
    f32 = jnp.float32
    bf16 = jnp.bfloat16

    own_dest = lax.dynamic_slice_in_dim(dest_sector, own_sec * sec_blocks, sec_blocks, 1)
    target = own_dest // sec_blocks
    peers = jnp.arange(sec_count, dtype=jnp.int32)
    send_hot = (target[:, :, None] == peers[None, None, :]).astype(bf16)
    chosen_left = jnp.einsum(
        "ask,asij->kisj", send_hot, left_env, preferred_element_type=f32
    ).astype(bf16)
    outgoing = jnp.einsum(
        "kisj,sjx->kix", chosen_left, wavefunction, preferred_element_type=f32
    ).astype(bf16)
    grid = dest_sector.reshape(left_count, sec_count, sec_blocks)
    mine = (grid // sec_blocks) == own_sec
    bond_hot = jnp.sum(mine, axis=2).T.astype(bf16)
    local_dest = jnp.sum(jnp.where(mine, grid % sec_blocks, 0), axis=(0, 2))
    dest_hot = local_dest[:, None] == jnp.arange(sec_blocks, dtype=jnp.int32)[None, :]
    item_ops = jnp.einsum(
        "ia,atpq->itpq", bond_hot, local_ops, preferred_element_type=f32
    ).astype(bf16)
    item_bond = jnp.einsum(
        "ia,at->it", bond_hot.astype(f32), right_bond.astype(f32)
    ).astype(jnp.int32)
    env_hot = (
        (item_bond[:, :, None, None] == jnp.arange(right_count, dtype=jnp.int32)[None, None, :, None])
        & dest_hot[:, None, None, :]
    ).astype(bf16)
    item_env = jnp.einsum(
        "itbd,bdmr->itmr", env_hot, right_env, preferred_element_type=f32
    ).astype(bf16)

    sector_env = jnp.einsum(
        "itmr,id->itdmr", item_env, dest_hot.astype(bf16), preferred_element_type=f32
    ).astype(bf16)

    chunk = rows // CHUNKS
    def process(received):
        incoming = received.reshape(sec_count, chunk, physical, rows)
        mixed = jnp.einsum(
            "itpq,ilqr->itlpr", item_ops, incoming, preferred_element_type=f32
        ).astype(bf16)
        return jnp.einsum("itlpr,itdmr->dlpm", mixed, sector_env, preferred_element_type=f32)

    def send(c):
        return lax.all_to_all(outgoing[:, c * chunk:(c + 1) * chunk], "sec", 0, 0, tiled=True)

    received = send(0)
    parts = []
    for c in range(CHUNKS):
        upcoming = None
        if c + 1 < CHUNKS:
            piece = outgoing[:, (c + 1) * chunk:(c + 2) * chunk]
            if parts:
                piece, parts[-1] = lax.optimization_barrier((piece, parts[-1]))
            upcoming = lax.all_to_all(piece, "sec", 0, 0, tiled=True)
        parts.append(process(received))
        received = upcoming
    partial_value = jnp.concatenate(parts, axis=1)
    share = rows // op_count
    pieces = partial_value.astype(bf16).reshape(sec_blocks, op_count, share, width)
    pieces = pieces.transpose(1, 0, 2, 3)
    gathered = lax.all_to_all(pieces, "op", 0, 0, tiled=True)
    summed = jnp.sum(gathered.astype(f32), axis=0)
    return summed.astype(bf16)


def solution(mesh):
    return jax.shard_map(
        body,
        mesh=mesh,
        in_specs=(
            P("sec", None, None),
            P("op", "sec", None, None),
            P("op", "sec", None, None),
            P("op", None, None, None),
            P("op", None),
            P("op", None),
        ),
        out_specs=P("sec", "op", None),
        check_vma=False,
    )
```

```python
import jax
import jax.numpy as jnp
from jax import lax
from jax.sharding import PartitionSpec as P


CHUNK_ROWS = (32, 16, 16)


def body(wavefunction, left_env, right_env, local_ops, dest_sector, right_bond):
    sec_blocks, rows, width = wavefunction.shape
    left_count = left_env.shape[0]
    right_count = right_env.shape[0]
    terms = local_ops.shape[1]
    physical = width // rows
    sec_count = lax.axis_size("sec")
    op_count = lax.axis_size("op")
    own_sec = lax.axis_index("sec")
    f32 = jnp.float32
    bf16 = jnp.bfloat16

    own_dest = lax.dynamic_slice_in_dim(dest_sector, own_sec * sec_blocks, sec_blocks, 1)
    target = own_dest // sec_blocks
    peers = jnp.arange(sec_count, dtype=jnp.int32)
    send_hot = (target[:, :, None] == peers[None, None, :]).astype(bf16)
    chosen_left = jnp.einsum(
        "ask,asij->kisj", send_hot, left_env, preferred_element_type=f32
    ).astype(bf16)
    outgoing = jnp.einsum(
        "kisj,sjx->kix", chosen_left, wavefunction, preferred_element_type=f32
    ).astype(bf16)
    grid = dest_sector.reshape(left_count, sec_count, sec_blocks)
    mine = (grid // sec_blocks) == own_sec
    bond_hot = jnp.sum(mine, axis=2).T.astype(bf16)
    local_dest = jnp.sum(jnp.where(mine, grid % sec_blocks, 0), axis=(0, 2))
    dest_hot = local_dest[:, None] == jnp.arange(sec_blocks, dtype=jnp.int32)[None, :]
    item_ops = jnp.einsum(
        "ia,atpq->itpq", bond_hot, local_ops, preferred_element_type=f32
    ).astype(bf16)
    item_bond = jnp.einsum(
        "ia,at->it", bond_hot.astype(f32), right_bond.astype(f32)
    ).astype(jnp.int32)
    env_hot = (
        (item_bond[:, :, None, None] == jnp.arange(right_count, dtype=jnp.int32)[None, None, :, None])
        & dest_hot[:, None, None, :]
    ).astype(bf16)
    item_env = jnp.einsum(
        "itbd,bdmr->itmr", env_hot, right_env, preferred_element_type=f32
    ).astype(bf16)

    sector_env = jnp.einsum(
        "itmr,id->itdmr", item_env, dest_hot.astype(bf16), preferred_element_type=f32
    ).astype(bf16)

    bounds = [0]
    for size in CHUNK_ROWS:
        bounds.append(bounds[-1] + size * rows // 64)

    def process(received):
        incoming = received.reshape(sec_count, -1, physical, rows)
        mixed = jnp.einsum(
            "itpq,ilqr->itlpr", item_ops, incoming, preferred_element_type=f32
        ).astype(bf16)
        return jnp.einsum("itlpr,itdmr->dlpm", mixed, sector_env, preferred_element_type=f32)

    count = len(CHUNK_ROWS)
    received = lax.all_to_all(outgoing[:, bounds[0]:bounds[1]], "sec", 0, 0, tiled=True)
    parts = []
    for c in range(count):
        upcoming = None
        if c + 1 < count:
            piece = outgoing[:, bounds[c + 1]:bounds[c + 2]]
            if parts:
                piece, received, parts[-1] = lax.optimization_barrier(
                    (piece, received, parts[-1])
                )
            else:
                piece, received = lax.optimization_barrier((piece, received))
            upcoming = lax.all_to_all(piece, "sec", 0, 0, tiled=True)
        parts.append(process(received))
        received = upcoming
    partial_value = jnp.concatenate(parts, axis=1)
    share = rows // op_count
    pieces = partial_value.astype(bf16).reshape(sec_blocks, op_count, share, width)
    pieces = pieces.transpose(1, 0, 2, 3)
    gathered = lax.all_to_all(pieces, "op", 0, 0, tiled=True)
    summed = jnp.sum(gathered.astype(f32), axis=0)
    return summed.astype(bf16)


def solution(mesh):
    return jax.shard_map(
        body,
        mesh=mesh,
        in_specs=(
            P("sec", None, None),
            P("op", "sec", None, None),
            P("op", "sec", None, None),
            P("op", None, None, None),
            P("op", None),
            P("op", None),
        ),
        out_specs=P("sec", "op", None),
        check_vma=False,
    )
```

```python
import jax
import jax.numpy as jnp
from jax import lax
from jax.sharding import PartitionSpec as P


CHUNK_ROWS = (48, 16)
PIECE_ROWS = 16


def body(wavefunction, left_env, right_env, local_ops, dest_sector, right_bond):
    sec_blocks, rows, width = wavefunction.shape
    left_count = left_env.shape[0]
    right_count = right_env.shape[0]
    terms = local_ops.shape[1]
    physical = width // rows
    sec_count = lax.axis_size("sec")
    op_count = lax.axis_size("op")
    own_sec = lax.axis_index("sec")
    f32 = jnp.float32
    bf16 = jnp.bfloat16

    own_dest = lax.dynamic_slice_in_dim(dest_sector, own_sec * sec_blocks, sec_blocks, 1)
    target = own_dest // sec_blocks
    peers = jnp.arange(sec_count, dtype=jnp.int32)
    send_hot = (target[:, :, None] == peers[None, None, :]).astype(bf16)
    chosen_left = jnp.einsum(
        "ask,asij->kisj", send_hot, left_env, preferred_element_type=f32
    ).astype(bf16)
    outgoing = jnp.einsum(
        "kisj,sjx->kix", chosen_left, wavefunction, preferred_element_type=f32
    ).astype(bf16)
    grid = dest_sector.reshape(left_count, sec_count, sec_blocks)
    mine = (grid // sec_blocks) == own_sec
    bond_hot = jnp.sum(mine, axis=2).T.astype(bf16)
    local_dest = jnp.sum(jnp.where(mine, grid % sec_blocks, 0), axis=(0, 2))
    dest_hot = local_dest[:, None] == jnp.arange(sec_blocks, dtype=jnp.int32)[None, :]
    item_ops = jnp.einsum(
        "ia,atpq->itpq", bond_hot, local_ops, preferred_element_type=f32
    ).astype(bf16)
    item_bond = jnp.einsum(
        "ia,at->it", bond_hot.astype(f32), right_bond.astype(f32)
    ).astype(jnp.int32)
    env_hot = (
        (item_bond[:, :, None, None] == jnp.arange(right_count, dtype=jnp.int32)[None, None, :, None])
        & dest_hot[:, None, None, :]
    ).astype(bf16)
    item_env = jnp.einsum(
        "itbd,bdmr->itmr", env_hot, right_env, preferred_element_type=f32
    ).astype(bf16)

    sector_env = jnp.einsum(
        "itmr,id->itdmr", item_env, dest_hot.astype(bf16), preferred_element_type=f32
    ).astype(bf16)

    bounds = [0]
    for size in CHUNK_ROWS:
        bounds.append(bounds[-1] + size * rows // 64)

    def process_piece(received):
        incoming = received.reshape(sec_count, -1, physical, rows)
        mixed = jnp.einsum(
            "itpq,ilqr->itlpr", item_ops, incoming, preferred_element_type=f32
        ).astype(bf16)
        return jnp.einsum("itlpr,itdmr->dlpm", mixed, sector_env, preferred_element_type=f32)

    def process(received):
        step = PIECE_ROWS * rows // 64
        return jnp.concatenate(
            [
                process_piece(received[:, start:start + step])
                for start in range(0, received.shape[1], step)
            ],
            axis=1,
        )

    count = len(CHUNK_ROWS)
    received = lax.all_to_all(outgoing[:, bounds[0]:bounds[1]], "sec", 0, 0, tiled=True)
    parts = []
    for c in range(count):
        upcoming = None
        if c + 1 < count:
            piece = outgoing[:, bounds[c + 1]:bounds[c + 2]]
            if parts:
                piece, received, parts[-1] = lax.optimization_barrier(
                    (piece, received, parts[-1])
                )
            else:
                piece, received = lax.optimization_barrier((piece, received))
            upcoming = lax.all_to_all(piece, "sec", 0, 0, tiled=True)
        parts.append(process(received))
        received = upcoming
    partial_value = jnp.concatenate(parts, axis=1)
    share = rows // op_count
    pieces = partial_value.astype(bf16).reshape(sec_blocks, op_count, share, width)
    pieces = pieces.transpose(1, 0, 2, 3)
    gathered = lax.all_to_all(pieces, "op", 0, 0, tiled=True)
    summed = jnp.sum(gathered.astype(f32), axis=0)
    return summed.astype(bf16)


def solution(mesh):
    return jax.shard_map(
        body,
        mesh=mesh,
        in_specs=(
            P("sec", None, None),
            P("op", "sec", None, None),
            P("op", "sec", None, None),
            P("op", None, None, None),
            P("op", None),
            P("op", None),
        ),
        out_specs=P("sec", "op", None),
        check_vma=False,
    )
```

```python
import jax
import jax.numpy as jnp
from jax import lax
from jax.sharding import PartitionSpec as P


CHUNK_ROWS = (40, 24)
PIECE_ROWS = 16


def body(wavefunction, left_env, right_env, local_ops, dest_sector, right_bond):
    sec_blocks, rows, width = wavefunction.shape
    left_count = left_env.shape[0]
    right_count = right_env.shape[0]
    terms = local_ops.shape[1]
    physical = width // rows
    sec_count = lax.axis_size("sec")
    op_count = lax.axis_size("op")
    own_sec = lax.axis_index("sec")
    f32 = jnp.float32
    bf16 = jnp.bfloat16

    own_dest = lax.dynamic_slice_in_dim(dest_sector, own_sec * sec_blocks, sec_blocks, 1)
    target = own_dest // sec_blocks
    peers = jnp.arange(sec_count, dtype=jnp.int32)
    send_hot = (target[:, :, None] == peers[None, None, :]).astype(bf16)
    chosen_left = jnp.einsum(
        "ask,asij->kisj", send_hot, left_env, preferred_element_type=f32
    ).astype(bf16)
    outgoing = jnp.einsum(
        "kisj,sjx->kix", chosen_left, wavefunction, preferred_element_type=f32
    ).astype(bf16)
    grid = dest_sector.reshape(left_count, sec_count, sec_blocks)
    mine = (grid // sec_blocks) == own_sec
    bond_hot = jnp.sum(mine, axis=2).T.astype(bf16)
    local_dest = jnp.sum(jnp.where(mine, grid % sec_blocks, 0), axis=(0, 2))
    dest_hot = local_dest[:, None] == jnp.arange(sec_blocks, dtype=jnp.int32)[None, :]
    item_ops = jnp.einsum(
        "ia,atpq->itpq", bond_hot, local_ops, preferred_element_type=f32
    ).astype(bf16)
    item_bond = jnp.einsum(
        "ia,at->it", bond_hot.astype(f32), right_bond.astype(f32)
    ).astype(jnp.int32)
    env_hot = (
        (item_bond[:, :, None, None] == jnp.arange(right_count, dtype=jnp.int32)[None, None, :, None])
        & dest_hot[:, None, None, :]
    ).astype(bf16)
    item_env = jnp.einsum(
        "itbd,bdmr->itmr", env_hot, right_env, preferred_element_type=f32
    ).astype(bf16)

    sector_env = jnp.einsum(
        "itmr,id->itdmr", item_env, dest_hot.astype(bf16), preferred_element_type=f32
    ).astype(bf16)

    bounds = [0]
    for size in CHUNK_ROWS:
        bounds.append(bounds[-1] + size * rows // 64)

    def process_piece(received):
        incoming = received.reshape(sec_count, -1, physical, rows)
        mixed = jnp.einsum(
            "itpq,ilqr->itlpr", item_ops, incoming, preferred_element_type=f32
        ).astype(bf16)
        return jnp.einsum("itlpr,itdmr->dlpm", mixed, sector_env, preferred_element_type=f32)

    def process(received):
        step = PIECE_ROWS * rows // 64
        return jnp.concatenate(
            [
                process_piece(received[:, start:start + step])
                for start in range(0, received.shape[1], step)
            ],
            axis=1,
        )

    count = len(CHUNK_ROWS)
    received = lax.all_to_all(outgoing[:, bounds[0]:bounds[1]], "sec", 0, 0, tiled=True)
    parts = []
    for c in range(count):
        upcoming = None
        if c + 1 < count:
            piece = outgoing[:, bounds[c + 1]:bounds[c + 2]]
            if parts:
                piece, received, parts[-1] = lax.optimization_barrier(
                    (piece, received, parts[-1])
                )
            else:
                piece, received = lax.optimization_barrier((piece, received))
            upcoming = lax.all_to_all(piece, "sec", 0, 0, tiled=True)
        parts.append(process(received))
        received = upcoming
    partial_value = jnp.concatenate(parts, axis=1)
    share = rows // op_count
    pieces = partial_value.astype(bf16).reshape(sec_blocks, op_count, share, width)
    pieces = pieces.transpose(1, 0, 2, 3)
    gathered = lax.all_to_all(pieces, "op", 0, 0, tiled=True)
    summed = jnp.sum(gathered.astype(f32), axis=0)
    return summed.astype(bf16)


def solution(mesh):
    return jax.shard_map(
        body,
        mesh=mesh,
        in_specs=(
            P("sec", None, None),
            P("op", "sec", None, None),
            P("op", "sec", None, None),
            P("op", None, None, None),
            P("op", None),
            P("op", None),
        ),
        out_specs=P("sec", "op", None),
        check_vma=False,
    )
```

```python
import jax
import jax.numpy as jnp
from jax import lax
from jax.sharding import PartitionSpec as P


CHUNK_ROWS = (48, 16)
PIECE_ROWS = 16


def body(wavefunction, left_env, right_env, local_ops, dest_sector, right_bond):
    sec_blocks, rows, width = wavefunction.shape
    left_count = left_env.shape[0]
    right_count = right_env.shape[0]
    terms = local_ops.shape[1]
    physical = width // rows
    sec_count = lax.axis_size("sec")
    op_count = lax.axis_size("op")
    own_sec = lax.axis_index("sec")
    f32 = jnp.float32
    bf16 = jnp.bfloat16

    own_dest = lax.dynamic_slice_in_dim(dest_sector, own_sec * sec_blocks, sec_blocks, 1)
    target = own_dest // sec_blocks
    peers = jnp.arange(sec_count, dtype=jnp.int32)
    send_hot = (target[:, :, None] == peers[None, None, :]).astype(bf16)
    chosen_left = jnp.einsum(
        "ask,asij->kisj", send_hot, left_env, preferred_element_type=f32
    ).astype(bf16)

    def outgoing(start, stop):
        return jnp.einsum(
            "kisj,sjx->kix",
            chosen_left[:, start:stop],
            wavefunction,
            preferred_element_type=f32,
        ).astype(bf16)

    grid = dest_sector.reshape(left_count, sec_count, sec_blocks)
    mine = (grid // sec_blocks) == own_sec
    bond_hot = jnp.sum(mine, axis=2).T.astype(bf16)
    local_dest = jnp.sum(jnp.where(mine, grid % sec_blocks, 0), axis=(0, 2))
    dest_hot = local_dest[:, None] == jnp.arange(sec_blocks, dtype=jnp.int32)[None, :]
    item_ops = jnp.einsum(
        "ia,atpq->itpq", bond_hot, local_ops, preferred_element_type=f32
    ).astype(bf16)
    item_bond = jnp.einsum(
        "ia,at->it", bond_hot.astype(f32), right_bond.astype(f32)
    ).astype(jnp.int32)
    env_hot = (
        (item_bond[:, :, None, None] == jnp.arange(right_count, dtype=jnp.int32)[None, None, :, None])
        & dest_hot[:, None, None, :]
    ).astype(bf16)
    item_env = jnp.einsum(
        "itbd,bdmr->itmr", env_hot, right_env, preferred_element_type=f32
    ).astype(bf16)

    sector_env = jnp.einsum(
        "itmr,id->itdmr", item_env, dest_hot.astype(bf16), preferred_element_type=f32
    ).astype(bf16)

    bounds = [0]
    for size in CHUNK_ROWS:
        bounds.append(bounds[-1] + size * rows // 64)

    def process_piece(received):
        incoming = received.reshape(sec_count, -1, physical, rows)
        mixed = jnp.einsum(
            "itpq,ilqr->itlpr", item_ops, incoming, preferred_element_type=f32
        ).astype(bf16)
        return jnp.einsum("itlpr,itdmr->dlpm", mixed, sector_env, preferred_element_type=f32)

    def process(received):
        step = PIECE_ROWS * rows // 64
        return jnp.concatenate(
            [
                process_piece(received[:, start:start + step])
                for start in range(0, received.shape[1], step)
            ],
            axis=1,
        )

    count = len(CHUNK_ROWS)
    received = lax.all_to_all(outgoing(bounds[0], bounds[1]), "sec", 0, 0, tiled=True)
    parts = []
    for c in range(count):
        upcoming = None
        if c + 1 < count:
            piece = outgoing(bounds[c + 1], bounds[c + 2])
            if parts:
                piece, received, parts[-1] = lax.optimization_barrier(
                    (piece, received, parts[-1])
                )
            else:
                piece, received = lax.optimization_barrier((piece, received))
            upcoming = lax.all_to_all(piece, "sec", 0, 0, tiled=True)
        parts.append(process(received))
        received = upcoming
    partial_value = jnp.concatenate(parts, axis=1)
    share = rows // op_count
    pieces = partial_value.astype(bf16).reshape(sec_blocks, op_count, share, width)
    pieces = pieces.transpose(1, 0, 2, 3)
    gathered = lax.all_to_all(pieces, "op", 0, 0, tiled=True)
    summed = jnp.sum(gathered.astype(f32), axis=0)
    return summed.astype(bf16)


def solution(mesh):
    return jax.shard_map(
        body,
        mesh=mesh,
        in_specs=(
            P("sec", None, None),
            P("op", "sec", None, None),
            P("op", "sec", None, None),
            P("op", None, None, None),
            P("op", None),
            P("op", None),
        ),
        out_specs=P("sec", "op", None),
        check_vma=False,
    )
```

```python
import jax
import jax.numpy as jnp
from jax import lax
from jax.sharding import PartitionSpec as P


CHUNK_ROWS = (48, 16)
PIECE_ROWS = 16


def body(wavefunction, left_env, right_env, local_ops, dest_sector, right_bond):
    sec_blocks, rows, width = wavefunction.shape
    left_count = left_env.shape[0]
    right_count = right_env.shape[0]
    terms = local_ops.shape[1]
    physical = width // rows
    sec_count = lax.axis_size("sec")
    op_count = lax.axis_size("op")
    own_sec = lax.axis_index("sec")
    f32 = jnp.float32
    bf16 = jnp.bfloat16

    own_dest = lax.dynamic_slice_in_dim(dest_sector, own_sec * sec_blocks, sec_blocks, 1)
    target = own_dest // sec_blocks
    peers = jnp.arange(sec_count, dtype=jnp.int32)
    send_hot = (target[:, :, None] == peers[None, None, :]).astype(bf16)
    chosen_left = jnp.einsum(
        "ask,asij->kisj", send_hot, left_env, preferred_element_type=f32
    ).astype(bf16)

    def outgoing(start, stop):
        return jnp.einsum(
            "kisj,sjx->kix",
            chosen_left[:, start:stop],
            wavefunction,
            preferred_element_type=f32,
        ).astype(bf16)

    grid = dest_sector.reshape(left_count, sec_count, sec_blocks)
    mine = (grid // sec_blocks) == own_sec
    bond_hot = jnp.sum(mine, axis=2).T.astype(bf16)
    local_dest = jnp.sum(jnp.where(mine, grid % sec_blocks, 0), axis=(0, 2))
    dest_hot = local_dest[:, None] == jnp.arange(sec_blocks, dtype=jnp.int32)[None, :]
    item_ops = jnp.einsum(
        "ia,atpq->itpq", bond_hot, local_ops, preferred_element_type=f32
    ).astype(bf16)
    item_bond = jnp.einsum(
        "ia,at->it", bond_hot.astype(f32), right_bond.astype(f32)
    ).astype(jnp.int32)
    env_hot = (
        (item_bond[:, :, None, None] == jnp.arange(right_count, dtype=jnp.int32)[None, None, :, None])
        & dest_hot[:, None, None, :]
    ).astype(bf16)
    item_env = jnp.einsum(
        "itbd,bdmr->itmr", env_hot, right_env, preferred_element_type=f32
    ).astype(bf16)

    sector_env = jnp.einsum(
        "itmr,id->itdmr", item_env, dest_hot.astype(bf16), preferred_element_type=f32
    ).astype(bf16)
    sector_matrix = sector_env.transpose(0, 1, 4, 2, 3).reshape(-1, sec_blocks * rows)

    bounds = [0]
    for size in CHUNK_ROWS:
        bounds.append(bounds[-1] + size * rows // 64)

    def process_piece(received):
        incoming = received.reshape(sec_count, -1, physical, rows)
        mixed = jnp.einsum(
            "itpq,ilqr->itlpr", item_ops, incoming, preferred_element_type=f32
        ).astype(bf16)
        piece_rows = mixed.shape[2]
        lhs = mixed.transpose(2, 3, 0, 1, 4).reshape(piece_rows * physical, -1)
        flat = jnp.dot(lhs, sector_matrix, preferred_element_type=f32)
        flat = flat.reshape(piece_rows, physical, sec_blocks, rows)
        return flat.transpose(2, 0, 1, 3)

    def process(received):
        step = PIECE_ROWS * rows // 64
        return jnp.concatenate(
            [
                process_piece(received[:, start:start + step])
                for start in range(0, received.shape[1], step)
            ],
            axis=1,
        )

    count = len(CHUNK_ROWS)
    received = lax.all_to_all(outgoing(bounds[0], bounds[1]), "sec", 0, 0, tiled=True)
    parts = []
    for c in range(count):
        upcoming = None
        if c + 1 < count:
            piece = outgoing(bounds[c + 1], bounds[c + 2])
            if parts:
                piece, received, parts[-1] = lax.optimization_barrier(
                    (piece, received, parts[-1])
                )
            else:
                piece, received = lax.optimization_barrier((piece, received))
            upcoming = lax.all_to_all(piece, "sec", 0, 0, tiled=True)
        parts.append(process(received))
        received = upcoming
    partial_value = jnp.concatenate(parts, axis=1)
    share = rows // op_count
    pieces = partial_value.astype(bf16).reshape(sec_blocks, op_count, share, width)
    pieces = pieces.transpose(1, 0, 2, 3)
    gathered = lax.all_to_all(pieces, "op", 0, 0, tiled=True)
    summed = jnp.sum(gathered.astype(f32), axis=0)
    return summed.astype(bf16)


def solution(mesh):
    return jax.shard_map(
        body,
        mesh=mesh,
        in_specs=(
            P("sec", None, None),
            P("op", "sec", None, None),
            P("op", "sec", None, None),
            P("op", None, None, None),
            P("op", None),
            P("op", None),
        ),
        out_specs=P("sec", "op", None),
        check_vma=False,
    )
```

```python
import jax
import jax.numpy as jnp
from jax import lax
from jax.sharding import PartitionSpec as P


CHUNK_ROWS = (48, 16)
PIECE_ROWS = 16


def body(wavefunction, left_env, right_env, local_ops, dest_sector, right_bond):
    sec_blocks, rows, width = wavefunction.shape
    left_count = left_env.shape[0]
    right_count = right_env.shape[0]
    terms = local_ops.shape[1]
    physical = width // rows
    sec_count = lax.axis_size("sec")
    op_count = lax.axis_size("op")
    own_sec = lax.axis_index("sec")
    f32 = jnp.float32
    bf16 = jnp.bfloat16

    own_dest = lax.dynamic_slice_in_dim(dest_sector, own_sec * sec_blocks, sec_blocks, 1)
    target = own_dest // sec_blocks
    peers = jnp.arange(sec_count, dtype=jnp.int32)
    send_hot = (target[:, :, None] == peers[None, None, :]).astype(bf16)
    chosen_left = jnp.einsum(
        "ask,asij->kisj", send_hot, left_env, preferred_element_type=f32
    ).astype(bf16)

    def outgoing(start, stop):
        return jnp.einsum(
            "kisj,sjx->kix",
            chosen_left[:, start:stop],
            wavefunction,
            preferred_element_type=f32,
        ).astype(bf16)

    grid = dest_sector.reshape(left_count, sec_count, sec_blocks)
    mine = (grid // sec_blocks) == own_sec
    bond_hot = jnp.sum(mine, axis=2).T.astype(bf16)
    local_dest = jnp.sum(jnp.where(mine, grid % sec_blocks, 0), axis=(0, 2))
    dest_hot = local_dest[:, None] == jnp.arange(sec_blocks, dtype=jnp.int32)[None, :]
    item_ops = jnp.einsum(
        "ia,atpq->itpq", bond_hot, local_ops, preferred_element_type=f32
    ).astype(bf16)
    item_bond = jnp.einsum(
        "ia,at->it", bond_hot.astype(f32), right_bond.astype(f32)
    ).astype(jnp.int32)
    env_hot = (
        (item_bond[:, :, None, None] == jnp.arange(right_count, dtype=jnp.int32)[None, None, :, None])
        & dest_hot[:, None, None, :]
    ).astype(bf16)
    item_env = jnp.einsum(
        "itbd,bdmr->itmr", env_hot, right_env, preferred_element_type=f32
    ).astype(bf16)

    sector_env = jnp.einsum(
        "itmr,id->itdmr", item_env, dest_hot.astype(bf16), preferred_element_type=f32
    ).astype(bf16)

    bounds = [0]
    for size in CHUNK_ROWS:
        bounds.append(bounds[-1] + size * rows // 64)

    def process_piece(received):
        incoming = received.reshape(sec_count, -1, physical, rows)
        mixed = jnp.einsum(
            "itpq,ilqr->itlpr", item_ops, incoming, preferred_element_type=f32
        ).astype(bf16)
        flat = jnp.einsum("itlpr,itdmr->lpdm", mixed, sector_env, preferred_element_type=f32)
        return flat.transpose(2, 0, 1, 3)

    def process(received):
        step = PIECE_ROWS * rows // 64
        return jnp.concatenate(
            [
                process_piece(received[:, start:start + step])
                for start in range(0, received.shape[1], step)
            ],
            axis=1,
        )

    count = len(CHUNK_ROWS)
    received = lax.all_to_all(outgoing(bounds[0], bounds[1]), "sec", 0, 0, tiled=True)
    parts = []
    for c in range(count):
        upcoming = None
        if c + 1 < count:
            piece = outgoing(bounds[c + 1], bounds[c + 2])
            if parts:
                piece, received, parts[-1] = lax.optimization_barrier(
                    (piece, received, parts[-1])
                )
            else:
                piece, received = lax.optimization_barrier((piece, received))
            upcoming = lax.all_to_all(piece, "sec", 0, 0, tiled=True)
        parts.append(process(received))
        received = upcoming
    partial_value = jnp.concatenate(parts, axis=1)
    share = rows // op_count
    pieces = partial_value.astype(bf16).reshape(sec_blocks, op_count, share, width)
    pieces = pieces.transpose(1, 0, 2, 3)
    gathered = lax.all_to_all(pieces, "op", 0, 0, tiled=True)
    summed = jnp.sum(gathered.astype(f32), axis=0)
    return summed.astype(bf16)


def solution(mesh):
    return jax.shard_map(
        body,
        mesh=mesh,
        in_specs=(
            P("sec", None, None),
            P("op", "sec", None, None),
            P("op", "sec", None, None),
            P("op", None, None, None),
            P("op", None),
            P("op", None),
        ),
        out_specs=P("sec", "op", None),
        check_vma=False,
    )
```

```python
import jax
import jax.numpy as jnp
from jax import lax
from jax.sharding import PartitionSpec as P


CHUNK_ROWS = (48, 16)
PIECE_ROWS = 16


def body(wavefunction, left_env, right_env, local_ops, dest_sector, right_bond):
    sec_blocks, rows, width = wavefunction.shape
    left_count = left_env.shape[0]
    right_count = right_env.shape[0]
    terms = local_ops.shape[1]
    physical = width // rows
    sec_count = lax.axis_size("sec")
    op_count = lax.axis_size("op")
    own_sec = lax.axis_index("sec")
    f32 = jnp.float32
    bf16 = jnp.bfloat16

    own_dest = lax.dynamic_slice_in_dim(dest_sector, own_sec * sec_blocks, sec_blocks, 1)
    target = own_dest // sec_blocks
    peers = jnp.arange(sec_count, dtype=jnp.int32)
    send_hot = (target[:, :, None] == peers[None, None, :]).astype(bf16)
    chosen_left = jnp.einsum(
        "ask,asij->kisj", send_hot, left_env, preferred_element_type=f32
    ).astype(bf16)

    def outgoing(start, stop):
        return jnp.einsum(
            "kisj,sjx->kix",
            chosen_left[:, start:stop],
            wavefunction,
            preferred_element_type=f32,
        ).astype(bf16)

    grid = dest_sector.reshape(left_count, sec_count, sec_blocks)
    mine = (grid // sec_blocks) == own_sec
    bond_hot = jnp.sum(mine, axis=2).T.astype(bf16)
    local_dest = jnp.sum(jnp.where(mine, grid % sec_blocks, 0), axis=(0, 2))
    dest_hot = local_dest[:, None] == jnp.arange(sec_blocks, dtype=jnp.int32)[None, :]
    item_ops = jnp.einsum(
        "ia,atpq->itpq", bond_hot, local_ops, preferred_element_type=f32
    ).astype(bf16)
    item_bond = jnp.einsum(
        "ia,at->it", bond_hot.astype(f32), right_bond.astype(f32)
    ).astype(jnp.int32)
    env_hot = (
        (item_bond[:, :, None, None] == jnp.arange(right_count, dtype=jnp.int32)[None, None, :, None])
        & dest_hot[:, None, None, :]
    ).astype(bf16)
    item_env = jnp.einsum(
        "itbd,bdmr->itmr", env_hot, right_env, preferred_element_type=f32
    ).astype(bf16)

    sector_env = jnp.einsum(
        "itmr,id->itdmr", item_env, dest_hot.astype(bf16), preferred_element_type=f32
    ).astype(bf16)

    bounds = [0]
    for size in CHUNK_ROWS:
        bounds.append(bounds[-1] + size * rows // 64)

    def process_piece(received):
        incoming = received.reshape(sec_count, -1, physical, rows)
        mixed = jnp.einsum(
            "itpq,ilqr->itlpr", item_ops, incoming, preferred_element_type=f32
        ).astype(bf16)
        mixed = lax.optimization_barrier(mixed)
        return jnp.einsum("itlpr,itdmr->dlpm", mixed, sector_env, preferred_element_type=f32)

    def process(received):
        step = PIECE_ROWS * rows // 64
        return jnp.concatenate(
            [
                process_piece(received[:, start:start + step])
                for start in range(0, received.shape[1], step)
            ],
            axis=1,
        )

    count = len(CHUNK_ROWS)
    received = lax.all_to_all(outgoing(bounds[0], bounds[1]), "sec", 0, 0, tiled=True)
    parts = []
    for c in range(count):
        upcoming = None
        if c + 1 < count:
            piece = outgoing(bounds[c + 1], bounds[c + 2])
            if parts:
                piece, received, parts[-1] = lax.optimization_barrier(
                    (piece, received, parts[-1])
                )
            else:
                piece, received = lax.optimization_barrier((piece, received))
            upcoming = lax.all_to_all(piece, "sec", 0, 0, tiled=True)
        parts.append(process(received))
        received = upcoming
    partial_value = jnp.concatenate(parts, axis=1)
    share = rows // op_count
    pieces = partial_value.astype(bf16).reshape(sec_blocks, op_count, share, width)
    pieces = pieces.transpose(1, 0, 2, 3)
    gathered = lax.all_to_all(pieces, "op", 0, 0, tiled=True)
    summed = jnp.sum(gathered.astype(f32), axis=0)
    return summed.astype(bf16)


def solution(mesh):
    return jax.shard_map(
        body,
        mesh=mesh,
        in_specs=(
            P("sec", None, None),
            P("op", "sec", None, None),
            P("op", "sec", None, None),
            P("op", None, None, None),
            P("op", None),
            P("op", None),
        ),
        out_specs=P("sec", "op", None),
        check_vma=False,
    )
```

```python
import jax
import jax.numpy as jnp
from jax import lax
from jax.sharding import PartitionSpec as P


CHUNK_ROWS = (48, 16)
PIECE_ROWS = 16


def body(wavefunction, left_env, right_env, local_ops, dest_sector, right_bond):
    sec_blocks, rows, width = wavefunction.shape
    left_count = left_env.shape[0]
    right_count = right_env.shape[0]
    terms = local_ops.shape[1]
    physical = width // rows
    sec_count = lax.axis_size("sec")
    op_count = lax.axis_size("op")
    own_sec = lax.axis_index("sec")
    f32 = jnp.float32
    bf16 = jnp.bfloat16

    own_dest = lax.dynamic_slice_in_dim(dest_sector, own_sec * sec_blocks, sec_blocks, 1)
    target = own_dest // sec_blocks
    peers = jnp.arange(sec_count, dtype=jnp.int32)
    send_hot = (target[:, :, None] == peers[None, None, :]).astype(bf16)
    chosen_left = jnp.einsum(
        "ask,asij->kisj", send_hot, left_env, preferred_element_type=f32
    ).astype(bf16)

    def outgoing(start, stop):
        return jnp.einsum(
            "kisj,sjx->kix",
            chosen_left[:, start:stop],
            wavefunction,
            preferred_element_type=f32,
        ).astype(bf16)

    grid = dest_sector.reshape(left_count, sec_count, sec_blocks)
    mine = (grid // sec_blocks) == own_sec
    bond_hot = jnp.sum(mine, axis=2).T.astype(bf16)
    local_dest = jnp.sum(jnp.where(mine, grid % sec_blocks, 0), axis=(0, 2))
    dest_hot = local_dest[:, None] == jnp.arange(sec_blocks, dtype=jnp.int32)[None, :]
    item_ops = jnp.einsum(
        "ia,atpq->itpq", bond_hot, local_ops, preferred_element_type=f32
    ).astype(bf16)
    item_bond = jnp.einsum(
        "ia,at->it", bond_hot.astype(f32), right_bond.astype(f32)
    ).astype(jnp.int32)
    env_hot = (
        (item_bond[:, :, None, None] == jnp.arange(right_count, dtype=jnp.int32)[None, None, :, None])
        & dest_hot[:, None, None, :]
    ).astype(bf16)
    item_env = jnp.einsum(
        "itbd,bdmr->itmr", env_hot, right_env, preferred_element_type=f32
    ).astype(bf16)

    sector_env = jnp.einsum(
        "itmr,id->itdmr", item_env, dest_hot.astype(bf16), preferred_element_type=f32
    ).astype(bf16)

    bounds = [0]
    for size in CHUNK_ROWS:
        bounds.append(bounds[-1] + size * rows // 64)

    def process_piece(received):
        incoming = received.reshape(sec_count, -1, physical, rows)
        mixed = jnp.einsum(
            "itpq,ilqr->itlpr", item_ops, incoming, preferred_element_type=f32
        ).astype(bf16)
        mixed = lax.optimization_barrier(mixed)
        return jnp.einsum("itlpr,itdmr->dlpm", mixed, sector_env, preferred_element_type=f32)

    def process(received):
        step = PIECE_ROWS * rows // 64
        count = received.shape[1] // step
        if count == 1:
            return process_piece(received)

        def one_piece(k, total):
            piece = lax.dynamic_slice_in_dim(received, k * step, step, 1)
            return lax.dynamic_update_slice_in_dim(total, process_piece(piece), k * step, 1)

        total = jnp.zeros((sec_blocks, received.shape[1], physical, rows), f32)
        return lax.fori_loop(0, count, one_piece, total)

    count = len(CHUNK_ROWS)
    received = lax.all_to_all(outgoing(bounds[0], bounds[1]), "sec", 0, 0, tiled=True)
    parts = []
    for c in range(count):
        upcoming = None
        if c + 1 < count:
            piece = outgoing(bounds[c + 1], bounds[c + 2])
            if parts:
                piece, received, parts[-1] = lax.optimization_barrier(
                    (piece, received, parts[-1])
                )
            else:
                piece, received = lax.optimization_barrier((piece, received))
            upcoming = lax.all_to_all(piece, "sec", 0, 0, tiled=True)
        parts.append(process(received))
        received = upcoming
    partial_value = jnp.concatenate(parts, axis=1)
    share = rows // op_count
    pieces = partial_value.astype(bf16).reshape(sec_blocks, op_count, share, width)
    pieces = pieces.transpose(1, 0, 2, 3)
    gathered = lax.all_to_all(pieces, "op", 0, 0, tiled=True)
    summed = jnp.sum(gathered.astype(f32), axis=0)
    return summed.astype(bf16)


def solution(mesh):
    return jax.shard_map(
        body,
        mesh=mesh,
        in_specs=(
            P("sec", None, None),
            P("op", "sec", None, None),
            P("op", "sec", None, None),
            P("op", None, None, None),
            P("op", None),
            P("op", None),
        ),
        out_specs=P("sec", "op", None),
        check_vma=False,
    )
```

```python
import jax
import jax.numpy as jnp
from jax import lax
from jax.sharding import PartitionSpec as P


CHUNK_ROWS = (48, 16)
PIECE_ROWS = 32


def body(wavefunction, left_env, right_env, local_ops, dest_sector, right_bond):
    sec_blocks, rows, width = wavefunction.shape
    left_count = left_env.shape[0]
    right_count = right_env.shape[0]
    terms = local_ops.shape[1]
    physical = width // rows
    sec_count = lax.axis_size("sec")
    op_count = lax.axis_size("op")
    own_sec = lax.axis_index("sec")
    f32 = jnp.float32
    bf16 = jnp.bfloat16

    own_dest = lax.dynamic_slice_in_dim(dest_sector, own_sec * sec_blocks, sec_blocks, 1)
    target = own_dest // sec_blocks
    peers = jnp.arange(sec_count, dtype=jnp.int32)
    send_hot = (target[:, :, None] == peers[None, None, :]).astype(bf16)
    chosen_left = jnp.einsum(
        "ask,asij->kisj", send_hot, left_env, preferred_element_type=f32
    ).astype(bf16)

    def outgoing(start, stop):
        return jnp.einsum(
            "kisj,sjx->kix",
            chosen_left[:, start:stop],
            wavefunction,
            preferred_element_type=f32,
        ).astype(bf16)

    grid = dest_sector.reshape(left_count, sec_count, sec_blocks)
    mine = (grid // sec_blocks) == own_sec
    bond_hot = jnp.sum(mine, axis=2).T.astype(bf16)
    local_dest = jnp.sum(jnp.where(mine, grid % sec_blocks, 0), axis=(0, 2))
    dest_hot = local_dest[:, None] == jnp.arange(sec_blocks, dtype=jnp.int32)[None, :]
    item_ops = jnp.einsum(
        "ia,atpq->itpq", bond_hot, local_ops, preferred_element_type=f32
    ).astype(bf16)
    item_bond = jnp.einsum(
        "ia,at->it", bond_hot.astype(f32), right_bond.astype(f32)
    ).astype(jnp.int32)
    env_hot = (
        (item_bond[:, :, None, None] == jnp.arange(right_count, dtype=jnp.int32)[None, None, :, None])
        & dest_hot[:, None, None, :]
    ).astype(bf16)
    item_env = jnp.einsum(
        "itbd,bdmr->itmr", env_hot, right_env, preferred_element_type=f32
    ).astype(bf16)

    sector_env = jnp.einsum(
        "itmr,id->itdmr", item_env, dest_hot.astype(bf16), preferred_element_type=f32
    ).astype(bf16)

    bounds = [0]
    for size in CHUNK_ROWS:
        bounds.append(bounds[-1] + size * rows // 64)

    def process_piece(received):
        incoming = received.reshape(sec_count, -1, physical, rows)
        mixed = jnp.einsum(
            "itpq,ilqr->itlpr", item_ops, incoming, preferred_element_type=f32
        ).astype(bf16)
        mixed = lax.optimization_barrier(mixed)
        return jnp.einsum("itlpr,itdmr->dlpm", mixed, sector_env, preferred_element_type=f32)

    def process(received):
        step = PIECE_ROWS * rows // 64
        return jnp.concatenate(
            [
                process_piece(received[:, start:start + step])
                for start in range(0, received.shape[1], step)
            ],
            axis=1,
        )

    count = len(CHUNK_ROWS)
    received = lax.all_to_all(outgoing(bounds[0], bounds[1]), "sec", 0, 0, tiled=True)
    parts = []
    for c in range(count):
        upcoming = None
        if c + 1 < count:
            piece = outgoing(bounds[c + 1], bounds[c + 2])
            if parts:
                piece, received, parts[-1] = lax.optimization_barrier(
                    (piece, received, parts[-1])
                )
            else:
                piece, received = lax.optimization_barrier((piece, received))
            upcoming = lax.all_to_all(piece, "sec", 0, 0, tiled=True)
        parts.append(process(received))
        received = upcoming
    partial_value = jnp.concatenate(parts, axis=1)
    share = rows // op_count
    pieces = partial_value.astype(bf16).reshape(sec_blocks, op_count, share, width)
    pieces = pieces.transpose(1, 0, 2, 3)
    gathered = lax.all_to_all(pieces, "op", 0, 0, tiled=True)
    summed = jnp.sum(gathered.astype(f32), axis=0)
    return summed.astype(bf16)


def solution(mesh):
    return jax.shard_map(
        body,
        mesh=mesh,
        in_specs=(
            P("sec", None, None),
            P("op", "sec", None, None),
            P("op", "sec", None, None),
            P("op", None, None, None),
            P("op", None),
            P("op", None),
        ),
        out_specs=P("sec", "op", None),
        check_vma=False,
    )
```

```python
import jax
import jax.numpy as jnp
from jax import lax
from jax.sharding import PartitionSpec as P


CHUNK_ROWS = (48, 16)
PIECE_ROWS = 16


def body(wavefunction, left_env, right_env, local_ops, dest_sector, right_bond):
    sec_blocks, rows, width = wavefunction.shape
    left_count = left_env.shape[0]
    right_count = right_env.shape[0]
    terms = local_ops.shape[1]
    physical = width // rows
    sec_count = lax.axis_size("sec")
    op_count = lax.axis_size("op")
    own_sec = lax.axis_index("sec")
    f32 = jnp.float32
    bf16 = jnp.bfloat16

    own_dest = lax.dynamic_slice_in_dim(dest_sector, own_sec * sec_blocks, sec_blocks, 1)
    target = own_dest // sec_blocks
    peers = jnp.arange(sec_count, dtype=jnp.int32)
    send_hot = (target[:, :, None] == peers[None, None, :]).astype(bf16)
    chosen_left = jnp.einsum(
        "ask,asij->kisj", send_hot, left_env, preferred_element_type=f32
    ).astype(bf16)

    def outgoing(start, stop):
        return jnp.einsum(
            "kisj,sjx->kix",
            chosen_left[:, start:stop],
            wavefunction,
            preferred_element_type=f32,
        ).astype(bf16)

    grid = dest_sector.reshape(left_count, sec_count, sec_blocks)
    mine = (grid // sec_blocks) == own_sec
    bond_hot = jnp.sum(mine, axis=2).T.astype(bf16)
    local_dest = jnp.sum(jnp.where(mine, grid % sec_blocks, 0), axis=(0, 2))
    dest_hot = local_dest[:, None] == jnp.arange(sec_blocks, dtype=jnp.int32)[None, :]
    item_ops = jnp.einsum(
        "ia,atpq->itpq", bond_hot, local_ops, preferred_element_type=f32
    ).astype(bf16)
    item_bond = jnp.einsum(
        "ia,at->it", bond_hot.astype(f32), right_bond.astype(f32)
    ).astype(jnp.int32)
    env_hot = (
        (item_bond[:, :, None, None] == jnp.arange(right_count, dtype=jnp.int32)[None, None, :, None])
        & dest_hot[:, None, None, :]
    ).astype(bf16)
    item_env = jnp.einsum(
        "itbd,bdmr->itmr", env_hot, right_env, preferred_element_type=f32
    ).astype(bf16)

    sector_env = jnp.einsum(
        "itmr,id->itdmr", item_env, dest_hot.astype(bf16), preferred_element_type=f32
    ).astype(bf16)

    bounds = [0]
    for size in CHUNK_ROWS:
        bounds.append(bounds[-1] + size * rows // 64)

    def process_piece(received, split=False):
        incoming = received.reshape(sec_count, -1, physical, rows)
        mixed = jnp.einsum(
            "itpq,ilqr->itlpr", item_ops, incoming, preferred_element_type=f32
        ).astype(bf16)
        if split:
            mixed = lax.optimization_barrier(mixed)
        return jnp.einsum("itlpr,itdmr->dlpm", mixed, sector_env, preferred_element_type=f32)

    def process(received):
        step = PIECE_ROWS * rows // 64
        return jnp.concatenate(
            [
                process_piece(received[:, start:start + step])
                for start in range(0, received.shape[1], step)
            ],
            axis=1,
        )

    count = len(CHUNK_ROWS)
    received = lax.all_to_all(outgoing(bounds[0], bounds[1]), "sec", 0, 0, tiled=True)
    parts = []
    for c in range(count):
        upcoming = None
        if c + 1 < count:
            piece = outgoing(bounds[c + 1], bounds[c + 2])
            if parts:
                piece, received, parts[-1] = lax.optimization_barrier(
                    (piece, received, parts[-1])
                )
            else:
                piece, received = lax.optimization_barrier((piece, received))
            upcoming = lax.all_to_all(piece, "sec", 0, 0, tiled=True)
        parts.append(process(received) if c + 1 < count else process_piece(received, True))
        received = upcoming
    partial_value = jnp.concatenate(parts, axis=1)
    share = rows // op_count
    pieces = partial_value.astype(bf16).reshape(sec_blocks, op_count, share, width)
    pieces = pieces.transpose(1, 0, 2, 3)
    gathered = lax.all_to_all(pieces, "op", 0, 0, tiled=True)
    summed = jnp.sum(gathered.astype(f32), axis=0)
    return summed.astype(bf16)


def solution(mesh):
    return jax.shard_map(
        body,
        mesh=mesh,
        in_specs=(
            P("sec", None, None),
            P("op", "sec", None, None),
            P("op", "sec", None, None),
            P("op", None, None, None),
            P("op", None),
            P("op", None),
        ),
        out_specs=P("sec", "op", None),
        check_vma=False,
    )
```

```python
import jax
import jax.numpy as jnp
from jax import lax
from jax.sharding import PartitionSpec as P


CHUNK_ROWS = (48, 16)
PIECE_ROWS = 16


def body(wavefunction, left_env, right_env, local_ops, dest_sector, right_bond):
    sec_blocks, rows, width = wavefunction.shape
    left_count = left_env.shape[0]
    right_count = right_env.shape[0]
    terms = local_ops.shape[1]
    physical = width // rows
    sec_count = lax.axis_size("sec")
    op_count = lax.axis_size("op")
    own_sec = lax.axis_index("sec")
    f32 = jnp.float32
    bf16 = jnp.bfloat16

    own_dest = lax.dynamic_slice_in_dim(dest_sector, own_sec * sec_blocks, sec_blocks, 1)
    target = own_dest // sec_blocks
    peers = jnp.arange(sec_count, dtype=jnp.int32)
    send_hot = (target[:, :, None] == peers[None, None, :]).astype(bf16)
    chosen_left = jnp.einsum(
        "ask,asij->kisj", send_hot, left_env, preferred_element_type=f32
    ).astype(bf16)

    def outgoing(start, stop):
        return jnp.einsum(
            "kisj,sjx->kix",
            chosen_left[:, start:stop],
            wavefunction,
            preferred_element_type=f32,
        ).astype(bf16)

    grid = dest_sector.reshape(left_count, sec_count, sec_blocks)
    mine = (grid // sec_blocks) == own_sec
    bond_hot = jnp.sum(mine, axis=2).T.astype(bf16)
    local_dest = jnp.sum(jnp.where(mine, grid % sec_blocks, 0), axis=(0, 2))
    dest_hot = local_dest[:, None] == jnp.arange(sec_blocks, dtype=jnp.int32)[None, :]
    item_ops = jnp.einsum(
        "ia,atpq->itpq", bond_hot, local_ops, preferred_element_type=f32
    ).astype(bf16)
    item_bond = jnp.einsum(
        "ia,at->it", bond_hot.astype(f32), right_bond.astype(f32)
    ).astype(jnp.int32)
    env_hot = (
        (item_bond[:, :, None, None] == jnp.arange(right_count, dtype=jnp.int32)[None, None, :, None])
        & dest_hot[:, None, None, :]
    ).astype(bf16)
    item_env = jnp.einsum(
        "itbd,bdmr->itmr", env_hot, right_env, preferred_element_type=f32
    ).astype(bf16)

    sector_env = jnp.einsum(
        "itmr,id->itdmr", item_env, dest_hot.astype(bf16), preferred_element_type=f32
    ).astype(bf16)

    bounds = [0]
    for size in CHUNK_ROWS:
        bounds.append(bounds[-1] + size * rows // 64)

    def process_piece(incoming):
        mixed = jnp.einsum(
            "itpq,ilqr->itlpr", item_ops, incoming, preferred_element_type=f32
        ).astype(bf16)
        return jnp.einsum("itlpr,itdmr->dlpm", mixed, sector_env, preferred_element_type=f32)

    def process(received):
        step = PIECE_ROWS * rows // 64
        incoming = received.reshape(sec_count, -1, physical, rows)
        return jnp.concatenate(
            [
                process_piece(incoming[:, start:start + step])
                for start in range(0, incoming.shape[1], step)
            ],
            axis=1,
        )

    count = len(CHUNK_ROWS)
    received = lax.all_to_all(outgoing(bounds[0], bounds[1]), "sec", 0, 0, tiled=True)
    parts = []
    for c in range(count):
        upcoming = None
        if c + 1 < count:
            piece = outgoing(bounds[c + 1], bounds[c + 2])
            if parts:
                piece, received, parts[-1] = lax.optimization_barrier(
                    (piece, received, parts[-1])
                )
            else:
                piece, received = lax.optimization_barrier((piece, received))
            upcoming = lax.all_to_all(piece, "sec", 0, 0, tiled=True)
        parts.append(process(received))
        received = upcoming
    partial_value = jnp.concatenate(parts, axis=1)
    share = rows // op_count
    pieces = partial_value.astype(bf16).reshape(sec_blocks, op_count, share, width)
    pieces = pieces.transpose(1, 0, 2, 3)
    gathered = lax.all_to_all(pieces, "op", 0, 0, tiled=True)
    summed = jnp.sum(gathered.astype(f32), axis=0)
    return summed.astype(bf16)


def solution(mesh):
    return jax.shard_map(
        body,
        mesh=mesh,
        in_specs=(
            P("sec", None, None),
            P("op", "sec", None, None),
            P("op", "sec", None, None),
            P("op", None, None, None),
            P("op", None),
            P("op", None),
        ),
        out_specs=P("sec", "op", None),
        check_vma=False,
    )
```

```python
import jax
import jax.numpy as jnp
from jax import lax
from jax.sharding import PartitionSpec as P


CHUNK_ROWS = (48, 16)
PIECE_ROWS = 48


def body(wavefunction, left_env, right_env, local_ops, dest_sector, right_bond):
    sec_blocks, rows, width = wavefunction.shape
    left_count = left_env.shape[0]
    right_count = right_env.shape[0]
    terms = local_ops.shape[1]
    physical = width // rows
    sec_count = lax.axis_size("sec")
    op_count = lax.axis_size("op")
    own_sec = lax.axis_index("sec")
    f32 = jnp.float32
    bf16 = jnp.bfloat16

    own_dest = lax.dynamic_slice_in_dim(dest_sector, own_sec * sec_blocks, sec_blocks, 1)
    target = own_dest // sec_blocks
    peers = jnp.arange(sec_count, dtype=jnp.int32)
    send_hot = (target[:, :, None] == peers[None, None, :]).astype(bf16)
    chosen_left = jnp.einsum(
        "ask,asij->kisj", send_hot, left_env, preferred_element_type=f32
    ).astype(bf16)

    def outgoing(start, stop):
        return jnp.einsum(
            "kisj,sjx->kix",
            chosen_left[:, start:stop],
            wavefunction,
            preferred_element_type=f32,
        ).astype(bf16)

    grid = dest_sector.reshape(left_count, sec_count, sec_blocks)
    mine = (grid // sec_blocks) == own_sec
    bond_hot = jnp.sum(mine, axis=2).T.astype(bf16)
    local_dest = jnp.sum(jnp.where(mine, grid % sec_blocks, 0), axis=(0, 2))
    dest_hot = local_dest[:, None] == jnp.arange(sec_blocks, dtype=jnp.int32)[None, :]
    item_ops = jnp.einsum(
        "ia,atpq->itpq", bond_hot, local_ops, preferred_element_type=f32
    ).astype(bf16)
    item_bond = jnp.einsum(
        "ia,at->it", bond_hot.astype(f32), right_bond.astype(f32)
    ).astype(jnp.int32)
    env_hot = (
        (item_bond[:, :, None, None] == jnp.arange(right_count, dtype=jnp.int32)[None, None, :, None])
        & dest_hot[:, None, None, :]
    ).astype(bf16)
    item_env = jnp.einsum(
        "itbd,bdmr->itmr", env_hot, right_env, preferred_element_type=f32
    ).astype(bf16)

    sector_env = jnp.einsum(
        "itmr,id->itdmr", item_env, dest_hot.astype(bf16), preferred_element_type=f32
    ).astype(bf16)

    bounds = [0]
    for size in CHUNK_ROWS:
        bounds.append(bounds[-1] + size * rows // 64)

    def process_piece(received):
        incoming = received.reshape(sec_count, -1, physical, rows)
        mixed = jnp.einsum(
            "itpq,ilqr->itlpr", item_ops, incoming, preferred_element_type=f32
        ).astype(bf16)
        return jnp.einsum("itlpr,itdmr->dlpm", mixed, sector_env, preferred_element_type=f32)

    def process(received):
        step = PIECE_ROWS * rows // 64
        return jnp.concatenate(
            [
                process_piece(received[:, start:start + step])
                for start in range(0, received.shape[1], step)
            ],
            axis=1,
        )

    count = len(CHUNK_ROWS)
    received = lax.all_to_all(outgoing(bounds[0], bounds[1]), "sec", 0, 0, tiled=True)
    parts = []
    for c in range(count):
        upcoming = None
        if c + 1 < count:
            piece = outgoing(bounds[c + 1], bounds[c + 2])
            if parts:
                piece, received, parts[-1] = lax.optimization_barrier(
                    (piece, received, parts[-1])
                )
            else:
                piece, received = lax.optimization_barrier((piece, received))
            upcoming = lax.all_to_all(piece, "sec", 0, 0, tiled=True)
        parts.append(process(received))
        received = upcoming
    partial_value = jnp.concatenate(parts, axis=1)
    share = rows // op_count
    pieces = partial_value.astype(bf16).reshape(sec_blocks, op_count, share, width)
    pieces = pieces.transpose(1, 0, 2, 3)
    gathered = lax.all_to_all(pieces, "op", 0, 0, tiled=True)
    summed = jnp.sum(gathered.astype(f32), axis=0)
    return summed.astype(bf16)


def solution(mesh):
    return jax.shard_map(
        body,
        mesh=mesh,
        in_specs=(
            P("sec", None, None),
            P("op", "sec", None, None),
            P("op", "sec", None, None),
            P("op", None, None, None),
            P("op", None),
            P("op", None),
        ),
        out_specs=P("sec", "op", None),
        check_vma=False,
    )
```
